512 devices in a mesh: clip: 64 (over x, y, z_hi, core), tm: 8 (over z_lo).
Axes of the slice: x: 4, y: 4, z: 16 (z_hi: 2, z_lo: 8; z = z_hi * 8 + z_lo), core: 2. Of those that a mesh axis runs over, the one named last changes fastest.
Arguments:
- clip_in: bfloat16 [64, 16, 32, 32, 128], P('clip', 'tm'), may hold values from -6 to 6
- cotangent: bfloat16 [64, 16, 32, 32, 128], P('clip', 'tm'), may hold values from -6 to 6
- spatial_w: bfloat16 [3, 3, 128, 128], replicated, may hold values from -0.1875 to 0.1875
- spatial_b: float32 [128], replicated, may hold values from -3 to 3
- temporal_w: bfloat16 [3, 128, 128], replicated, may hold values from -0.3125 to 0.3125
Outputs:
- grad_input: bfloat16 [64, 16, 32, 32, 128], P('clip', 'tm')
- grad_spatial_w: float32 [3, 3, 128, 128], replicated
- grad_spatial_b: float32 [128], replicated
- grad_temporal_w: float32 [3, 128, 128], replicated
The draws below stay inside these ranges and needn't reach their ends.
All inputs are finite; a program needn't handle non-finite values.
Results may differ from the reference program's by a relative error of at most 0.006.
Values may be sent and summed in bfloat16 or wider, within the bound.
No kernel may reach another device: no remote copies, remote signals or barrier semaphores. Data moves between devices by JAX's collectives and lax.ppermute only.
A program may use at most 64 MiB of HBM per device.

```python
import jax
import jax.numpy as jnp
from jax import lax

C = 128
W = 32
T_SIZE = 16
H = 32
CLIPS = 64


def steps_of(stream_key, dims, cuts, low, top_value):
    loudness, own = 1.0, jax.random.fold_in(stream_key, 6)
    for dim, blocks in cuts:
        heights = jnp.exp(jax.random.uniform(jax.random.fold_in(own, dim), (blocks,), jnp.float32, low / len(cuts), top_value / len(cuts)))
        loudness = loudness * jnp.repeat(heights, dims[dim] // blocks).reshape([-1 if axis == dim else 1 for axis in range(len(dims))])
    return loudness


def normal_values(key, extent, scale, most, cuts=(), kind=jnp.bfloat16):
    entries = scale * jax.random.normal(key, extent, jnp.float32)
    if cuts:
        entries = entries * steps_of(key, extent, cuts, -0.22, 0.18)
    return jnp.clip(entries, -most, most).astype(kind)


def setup_inputs(seed: int = 0) -> dict:
    key_list = jax.random.split(jax.random.key(seed), 6)
    clip_in = normal_values(key_list[0], (CLIPS, T_SIZE, H, W, C), 1.0, 6.0, ((0, 64), (1, 8)))
    cotangent = normal_values(key_list[1], (CLIPS, T_SIZE, H, W, C), 1.0, 6.0, ((0, 64), (1, 8)))
    spatial_w = normal_values(key_list[2], (3, 3, C, C), (9 * C) ** -0.5, 0.1875)
    spatial_b = normal_values(key_list[3], (C,), 0.7, 3.0, (), jnp.float32)
    temporal_w = normal_values(key_list[4], (3, C, C), (3 * C) ** -0.5, 0.3125)
    return {"clip_in": clip_in, "cotangent": cotangent, "spatial_w": spatial_w, "spatial_b": spatial_b, "temporal_w": temporal_w}


def spatial_forward(frames, weights, bias):
    count, height, width, chan = frames.shape
    padded = jnp.pad(frames, ((0, 0), (1, 1), (1, 1), (0, 0)))
    total = jnp.zeros((count * height * width, chan), jnp.float32)
    for i in range(3):
        for j in range(3):
            window = padded[:, i:i + height, j:j + width, :].reshape(-1, chan)
            total = total + jnp.dot(window, weights[i, j], preferred_element_type=jnp.float32)
    return (total + bias).reshape(count, height, width, chan)

def spatial_transpose(grads, weights):
    count, height, width, chan = grads.shape
    padded = jnp.pad(grads, ((0, 0), (1, 1), (1, 1), (0, 0)))
    total = jnp.zeros((count * height * width, chan), jnp.float32)
    for i in range(3):
        for j in range(3):
            window = padded[:, 2 - i:2 - i + height, 2 - j:2 - j + width, :].reshape(-1, chan)
            total = total + jnp.dot(window, weights[i, j].T, preferred_element_type=jnp.float32)
    return total.reshape(count, height, width, chan)

def spatial_weight_grad(frames, grads):
    count, height, width, chan = frames.shape
    padded = jnp.pad(frames, ((0, 0), (1, 1), (1, 1), (0, 0)))
    flat_grads = grads.reshape(-1, chan)
    result = []
    for i in range(3):
        row_terms = []
        for j in range(3):
            window = padded[:, i:i + height, j:j + width, :].reshape(-1, chan)
            row_terms.append(lax.dot_general(window, flat_grads, (((0,), (0,)), ((), ())), preferred_element_type=jnp.float32))
        result.append(jnp.stack(row_terms))
    return jnp.stack(result)

def one_clip(pieces, spatial_w, spatial_b, temporal_w):
    frames, cot = pieces
    count, height, width, chan = frames.shape
    pre = spatial_forward(frames, spatial_w, spatial_b)
    act = jax.nn.silu(pre).astype(jnp.bfloat16)
    later = jnp.concatenate([cot, jnp.zeros((2, height, width, chan), cot.dtype)], axis=0)
    earlier = jnp.concatenate([jnp.zeros((2, height, width, chan), act.dtype), act], axis=0)
    flat_cot = cot.reshape(-1, chan)
    grad_act = jnp.zeros((count * height * width, chan), jnp.float32)
    lag_terms = []
    for k in range(3):
        grad_act = grad_act + jnp.dot(later[k:k + count].reshape(-1, chan), temporal_w[k].T, preferred_element_type=jnp.float32)
        shifted = earlier[2 - k:2 - k + count].reshape(-1, chan)
        lag_terms.append(lax.dot_general(shifted, flat_cot, (((0,), (0,)), ((), ())), preferred_element_type=jnp.float32))
    grad_act = grad_act.astype(jnp.bfloat16).reshape(count, height, width, chan)
    sig = jax.nn.sigmoid(pre)
    grad_pre = (grad_act.astype(jnp.float32) * sig * (1.0 + pre * (1.0 - sig))).astype(jnp.bfloat16)
    grad_in = (cot.astype(jnp.float32) + spatial_transpose(grad_pre, spatial_w)).astype(jnp.bfloat16)
    grad_sw = spatial_weight_grad(frames, grad_pre)
    grad_sb = lax.optimization_barrier(jnp.sum(grad_pre.astype(jnp.float32).reshape(-1, chan), axis=0))
    return (grad_in, grad_sw, grad_sb, jnp.stack(lag_terms))

def reference(clip_in, cotangent, spatial_w, spatial_b, temporal_w):

    def work(pieces):
        return one_clip(pieces, spatial_w, spatial_b, temporal_w)
    grad_in, grad_sw, grad_sb, grad_tw = lax.map(work, (clip_in, cotangent))
    norm = 1.0 / jnp.sqrt(jnp.float32(CLIPS * T_SIZE * H * W))
    return (grad_in, lax.optimization_barrier(jnp.sum(grad_sw, axis=0)) * norm, lax.optimization_barrier(jnp.sum(grad_sb, axis=0)) * norm, lax.optimization_barrier(jnp.sum(grad_tw, axis=0)) * norm)
```

```python
import jax
import jax.numpy as jnp
from jax import lax
from jax.sharding import PartitionSpec as P

GRAY4 = (0, 1, 3, 2)


def spatial_forward(frames, weights, bias):
    count, height, width, chan = frames.shape
    padded = jnp.pad(frames, ((0, 0), (1, 1), (1, 1), (0, 0)))
    total = jnp.zeros((count * height * width, chan), jnp.float32)
    for i in range(3):
        for j in range(3):
            window = padded[:, i : i + height, j : j + width, :].reshape(-1, chan)
            total = total + jnp.dot(window, weights[i, j], preferred_element_type=jnp.float32)
    return (total + bias).reshape(count, height, width, chan)


def spatial_transpose(grads, weights):
    count, height, width, chan = grads.shape
    padded = jnp.pad(grads, ((0, 0), (1, 1), (1, 1), (0, 0)))
    total = jnp.zeros((count * height * width, chan), jnp.float32)
    for i in range(3):
        for j in range(3):
            window = padded[:, 2 - i : 2 - i + height, 2 - j : 2 - j + width, :].reshape(-1, chan)
            total = total + jnp.dot(window, weights[i, j].T, preferred_element_type=jnp.float32)
    return total.reshape(count, height, width, chan)


def spatial_weight_grad(frames, grads):
    count, height, width, chan = frames.shape
    padded = jnp.pad(frames, ((0, 0), (1, 1), (1, 1), (0, 0)))
    flat_grads = grads.reshape(-1, chan)
    result = []
    for i in range(3):
        row_terms = []
        for j in range(3):
            window = padded[:, i : i + height, j : j + width, :].reshape(-1, chan)
            row_terms.append(
                lax.dot_general(
                    window, flat_grads, (((0,), (0,)), ((), ())), preferred_element_type=jnp.float32
                )
            )
        result.append(jnp.stack(row_terms))
    return jnp.stack(result)


def temporal_back(act, later, temporal_w):
    count, height, width, chan = act.shape
    flat_act = act.reshape(-1, chan)
    grad_act = jnp.zeros((count * height * width, chan), jnp.float32)
    lag_terms = []
    for k in range(3):
        window = later[k : k + count].reshape(-1, chan)
        grad_act = grad_act + jnp.dot(window, temporal_w[k].T, preferred_element_type=jnp.float32)
        lag_terms.append(
            lax.dot_general(
                flat_act, window, (((0,), (0,)), ((), ())), preferred_element_type=jnp.float32
            )
        )
    grad_act = grad_act.astype(jnp.bfloat16).reshape(count, height, width, chan)
    return grad_act, jnp.stack(lag_terms)


def butterfly_steps(n_clip, n_tm):
    n_x = n_clip // 16
    steps = []

    def clip_step(field, size, stride, labels, bit, halve):
        perm, bits = [], []
        pos = {lab: r for r, lab in enumerate(labels)}
        for c in range(n_clip):
            r = (c // stride) % size
            lab = labels[r]
            r2 = pos[lab ^ (1 << bit)]
            perm.append((c, c + (r2 - r) * stride))
            bits.append((lab >> bit) & 1)
        steps.append(("clip", tuple(perm), tuple(bits), halve))

    clip_step("core", 2, 1, (0, 1), 0, True)
    for b in range(2):
        clip_step("x", n_x, 16, GRAY4, b, True)
    for b in range(2):
        clip_step("y", 4, 4, GRAY4, b, False)
    clip_step("zh", 2, 2, (0, 1), 0, False)
    b = 0
    while (1 << b) < n_tm:
        perm = tuple((t, t ^ (1 << b)) for t in range(n_tm))
        bits = tuple((t >> b) & 1 for t in range(n_tm))
        steps.append(("tm", perm, bits, False))
        b += 1
    return steps


def all_reduce(x, n_clip, n_tm):
    steps = butterfly_steps(n_clip, n_tm)
    halved = []
    for axis, perm, bits, halve in steps:
        if halve:
            bit = jnp.asarray(bits, jnp.int32)[lax.axis_index(axis)]
            h = x.shape[0] // 2
            keep = lax.dynamic_slice_in_dim(x, bit * h, h)
            send = lax.dynamic_slice_in_dim(x, (1 - bit) * h, h)
            x = keep + lax.ppermute(send, axis, perm)
            halved.append((axis, perm, bits))
        else:
            x = x + lax.ppermute(x, axis, perm)
    for axis, perm, bits in halved[::-1]:
        bit = jnp.asarray(bits, jnp.int32)[lax.axis_index(axis)]
        other = lax.ppermute(x, axis, perm)
        both = jnp.stack([x, other])
        first = lax.dynamic_index_in_dim(both, bit, keepdims=False)
        second = lax.dynamic_index_in_dim(both, 1 - bit, keepdims=False)
        x = jnp.concatenate([first, second], 0)
    return x


def local(clip_in, cotangent, spatial_w, spatial_b, temporal_w):
    frames = clip_in[0]
    cot = cotangent[0]
    count, height, width, chan = frames.shape
    n_tm = lax.axis_size("tm")
    n_clip = lax.axis_size("clip")
    after = lax.ppermute(cot, "tm", [(t, t - 1) for t in range(1, n_tm)])
    pre = spatial_forward(frames, spatial_w, spatial_b)
    act = jax.nn.silu(pre).astype(jnp.bfloat16)
    later = jnp.concatenate([cot, after], axis=0)
    grad_act, grad_tw = temporal_back(act, later, temporal_w)
    sig = jax.nn.sigmoid(pre)
    grad_pre = (grad_act.astype(jnp.float32) * sig * (1.0 + pre * (1.0 - sig))).astype(jnp.bfloat16)
    grad_in = (cot.astype(jnp.float32) + spatial_transpose(grad_pre, spatial_w)).astype(
        jnp.bfloat16
    )
    grad_sw = spatial_weight_grad(frames, grad_pre)
    grad_sb = jnp.sum(grad_pre.astype(jnp.float32).reshape(-1, chan), axis=0)
    n_sw = 9 * chan
    n_tw = 3 * chan
    rows = n_sw + n_tw + 1
    quantum = 64
    padded_rows = -(-rows // quantum) * quantum
    packed = jnp.concatenate(
        [
            grad_sw.reshape(n_sw, chan),
            grad_tw.reshape(n_tw, chan),
            grad_sb[None],
            jnp.zeros((padded_rows - rows, chan), jnp.float32),
        ],
        axis=0,
    )
    total = all_reduce(packed, n_clip, n_tm)
    total_cells = n_clip * count * n_tm * height * width
    norm = 1.0 / jnp.sqrt(jnp.float32(total_cells))
    out_sw = total[:n_sw].reshape(3, 3, chan, chan) * norm
    out_tw = total[n_sw : n_sw + n_tw].reshape(3, chan, chan) * norm
    out_sb = total[n_sw + n_tw] * norm
    return (grad_in[None], out_sw, out_sb, out_tw)


def solution(mesh):
    in_specs = (P("clip", "tm", None, None, None), P("clip", "tm", None, None, None), P(), P(), P())
    out_specs = (P("clip", "tm", None, None, None), P(), P(), P())
    return jax.shard_map(local, mesh=mesh, in_specs=in_specs, out_specs=out_specs, check_vma=False)
```

```python
import jax
import jax.numpy as jnp
from jax import lax
from jax.sharding import PartitionSpec as P

GRAY4 = (0, 1, 3, 2)


CONV_DIMS = ("NHWC", "HWIO", "NHWC")


def spatial_forward(frames, weights, bias):
    total = lax.conv_general_dilated(
        frames, weights, (1, 1), ((1, 1), (1, 1)), dimension_numbers=CONV_DIMS,
        preferred_element_type=jnp.float32,
    )
    return total + bias


def spatial_transpose(grads, weights):
    flipped = jnp.transpose(weights[::-1, ::-1], (0, 1, 3, 2))
    return lax.conv_general_dilated(
        grads, flipped, (1, 1), ((1, 1), (1, 1)), dimension_numbers=CONV_DIMS,
        preferred_element_type=jnp.float32,
    )


def spatial_weight_grad(frames, grads):
    result = lax.conv_general_dilated(
        frames, grads, (1, 1), ((1, 1), (1, 1)), dimension_numbers=("CHWN", "IHWO", "NHWC"),
        preferred_element_type=jnp.float32,
    )
    return jnp.transpose(result, (1, 2, 0, 3))


def temporal_back(act, later, temporal_w):
    count, height, width, chan = act.shape
    flat_act = act.reshape(-1, chan)
    grad_act = jnp.zeros((count * height * width, chan), jnp.float32)
    lag_terms = []
    for k in range(3):
        window = later[k : k + count].reshape(-1, chan)
        grad_act = grad_act + jnp.dot(window, temporal_w[k].T, preferred_element_type=jnp.float32)
        lag_terms.append(
            lax.dot_general(
                flat_act, window, (((0,), (0,)), ((), ())), preferred_element_type=jnp.float32
            )
        )
    grad_act = grad_act.astype(jnp.bfloat16).reshape(count, height, width, chan)
    return grad_act, jnp.stack(lag_terms)


def butterfly_steps(n_clip, n_tm):
    n_x = n_clip // 16
    steps = []

    def clip_step(field, size, stride, labels, bit, halve):
        perm, bits = [], []
        pos = {lab: r for r, lab in enumerate(labels)}
        for c in range(n_clip):
            r = (c // stride) % size
            lab = labels[r]
            r2 = pos[lab ^ (1 << bit)]
            perm.append((c, c + (r2 - r) * stride))
            bits.append((lab >> bit) & 1)
        steps.append(("clip", tuple(perm), tuple(bits), halve))

    clip_step("core", 2, 1, (0, 1), 0, True)
    for b in range(2):
        clip_step("x", n_x, 16, GRAY4, b, True)
    for b in range(2):
        clip_step("y", 4, 4, GRAY4, b, False)
    clip_step("zh", 2, 2, (0, 1), 0, False)
    b = 0
    while (1 << b) < n_tm:
        perm = tuple((t, t ^ (1 << b)) for t in range(n_tm))
        bits = tuple((t >> b) & 1 for t in range(n_tm))
        steps.append(("tm", perm, bits, False))
        b += 1
    return steps


def all_reduce(x, n_clip, n_tm):
    steps = butterfly_steps(n_clip, n_tm)
    halved = []
    for axis, perm, bits, halve in steps:
        if halve:
            bit = jnp.asarray(bits, jnp.int32)[lax.axis_index(axis)]
            h = x.shape[0] // 2
            keep = lax.dynamic_slice_in_dim(x, bit * h, h)
            send = lax.dynamic_slice_in_dim(x, (1 - bit) * h, h)
            x = keep + lax.ppermute(send, axis, perm)
            halved.append((axis, perm, bits))
        else:
            x = x + lax.ppermute(x, axis, perm)
    for axis, perm, bits in halved[::-1]:
        bit = jnp.asarray(bits, jnp.int32)[lax.axis_index(axis)]
        other = lax.ppermute(x, axis, perm)
        both = jnp.stack([x, other])
        first = lax.dynamic_index_in_dim(both, bit, keepdims=False)
        second = lax.dynamic_index_in_dim(both, 1 - bit, keepdims=False)
        x = jnp.concatenate([first, second], 0)
    return x


def local(clip_in, cotangent, spatial_w, spatial_b, temporal_w):
    frames = clip_in[0]
    cot = cotangent[0]
    count, height, width, chan = frames.shape
    n_tm = lax.axis_size("tm")
    n_clip = lax.axis_size("clip")
    after = lax.ppermute(cot, "tm", [(t, t - 1) for t in range(1, n_tm)])
    pre = spatial_forward(frames, spatial_w, spatial_b)
    act = jax.nn.silu(pre).astype(jnp.bfloat16)
    later = jnp.concatenate([cot, after], axis=0)
    grad_act, grad_tw = temporal_back(act, later, temporal_w)
    sig = jax.nn.sigmoid(pre)
    grad_pre = (grad_act.astype(jnp.float32) * sig * (1.0 + pre * (1.0 - sig))).astype(jnp.bfloat16)
    grad_in = (cot.astype(jnp.float32) + spatial_transpose(grad_pre, spatial_w)).astype(
        jnp.bfloat16
    )
    grad_sw = spatial_weight_grad(frames, grad_pre)
    grad_sb = jnp.sum(grad_pre.astype(jnp.float32).reshape(-1, chan), axis=0)
    n_sw = 9 * chan
    n_tw = 3 * chan
    rows = n_sw + n_tw + 1
    quantum = 64
    padded_rows = -(-rows // quantum) * quantum
    packed = jnp.concatenate(
        [
            grad_sw.reshape(n_sw, chan),
            grad_tw.reshape(n_tw, chan),
            grad_sb[None],
            jnp.zeros((padded_rows - rows, chan), jnp.float32),
        ],
        axis=0,
    )
    total = all_reduce(packed, n_clip, n_tm)
    total_cells = n_clip * count * n_tm * height * width
    norm = 1.0 / jnp.sqrt(jnp.float32(total_cells))
    out_sw = total[:n_sw].reshape(3, 3, chan, chan) * norm
    out_tw = total[n_sw : n_sw + n_tw].reshape(3, chan, chan) * norm
    out_sb = total[n_sw + n_tw] * norm
    return (grad_in[None], out_sw, out_sb, out_tw)


def solution(mesh):
    in_specs = (P("clip", "tm", None, None, None), P("clip", "tm", None, None, None), P(), P(), P())
    out_specs = (P("clip", "tm", None, None, None), P(), P(), P())
    return jax.shard_map(local, mesh=mesh, in_specs=in_specs, out_specs=out_specs, check_vma=False)
```

```python
import jax
import jax.numpy as jnp
from jax import lax
from jax.sharding import PartitionSpec as P

GRAY4 = (0, 1, 3, 2)


CONV_DIMS = ("NHWC", "HWIO", "NHWC")


def spatial_forward(frames, weights, bias):
    total = lax.conv_general_dilated(
        frames, weights, (1, 1), ((1, 1), (1, 1)), dimension_numbers=CONV_DIMS,
        preferred_element_type=jnp.float32,
    )
    return total + bias


def spatial_transpose(grads, weights):
    flipped = jnp.transpose(weights[::-1, ::-1], (0, 1, 3, 2))
    return lax.conv_general_dilated(
        grads, flipped, (1, 1), ((1, 1), (1, 1)), dimension_numbers=CONV_DIMS,
        preferred_element_type=jnp.float32,
    )


def spatial_weight_grad(frames, grads):
    result = lax.conv_general_dilated(
        frames, grads, (1, 1), ((1, 1), (1, 1)), dimension_numbers=("CHWN", "IHWO", "NHWC"),
        preferred_element_type=jnp.float32,
    )
    return jnp.transpose(result, (1, 2, 0, 3))


def temporal_back(act, later, temporal_w):
    count, height, width, chan = act.shape
    flat_act = act.reshape(-1, chan)
    grad_act = jnp.zeros((count * height * width, chan), jnp.float32)
    lag_terms = []
    for k in range(3):
        window = later[k : k + count].reshape(-1, chan)
        grad_act = grad_act + jnp.dot(window, temporal_w[k].T, preferred_element_type=jnp.float32)
        lag_terms.append(
            lax.dot_general(
                flat_act, window, (((0,), (0,)), ((), ())), preferred_element_type=jnp.float32
            )
        )
    grad_act = grad_act.astype(jnp.bfloat16).reshape(count, height, width, chan)
    return grad_act, jnp.stack(lag_terms)


def butterfly_steps(n_clip, n_tm):
    n_x = n_clip // 16
    steps = []

    def clip_step(field, size, stride, labels, bit, halve):
        perm, bits = [], []
        pos = {lab: r for r, lab in enumerate(labels)}
        for c in range(n_clip):
            r = (c // stride) % size
            lab = labels[r]
            r2 = pos[lab ^ (1 << bit)]
            perm.append((c, c + (r2 - r) * stride))
            bits.append((lab >> bit) & 1)
        steps.append(("clip", tuple(perm), tuple(bits), halve))

    clip_step("core", 2, 1, (0, 1), 0, True)
    for b in range(2):
        clip_step("x", n_x, 16, GRAY4, b, True)
    for b in range(2):
        clip_step("y", 4, 4, GRAY4, b, True)
    clip_step("zh", 2, 2, (0, 1), 0, False)
    b = 0
    while (1 << b) < n_tm:
        perm = tuple((t, t ^ (1 << b)) for t in range(n_tm))
        bits = tuple((t >> b) & 1 for t in range(n_tm))
        steps.append(("tm", perm, bits, False))
        b += 1
    return steps


def all_reduce(x, n_clip, n_tm):
    steps = butterfly_steps(n_clip, n_tm)
    halved = []
    for axis, perm, bits, halve in steps:
        if halve:
            bit = jnp.asarray(bits, jnp.int32)[lax.axis_index(axis)]
            h = x.shape[0] // 2
            keep = lax.dynamic_slice_in_dim(x, bit * h, h)
            send = lax.dynamic_slice_in_dim(x, (1 - bit) * h, h)
            x = keep + lax.ppermute(send, axis, perm)
            halved.append((axis, perm, bits))
        else:
            x = x + lax.ppermute(x, axis, perm)
    for axis, perm, bits in halved[::-1]:
        bit = jnp.asarray(bits, jnp.int32)[lax.axis_index(axis)]
        other = lax.ppermute(x, axis, perm)
        both = jnp.stack([x, other])
        first = lax.dynamic_index_in_dim(both, bit, keepdims=False)
        second = lax.dynamic_index_in_dim(both, 1 - bit, keepdims=False)
        x = jnp.concatenate([first, second], 0)
    return x


def local(clip_in, cotangent, spatial_w, spatial_b, temporal_w):
    frames = clip_in[0]
    cot = cotangent[0]
    count, height, width, chan = frames.shape
    n_tm = lax.axis_size("tm")
    n_clip = lax.axis_size("clip")
    after = lax.ppermute(cot, "tm", [(t, t - 1) for t in range(1, n_tm)])
    pre = spatial_forward(frames, spatial_w, spatial_b)
    act = jax.nn.silu(pre).astype(jnp.bfloat16)
    later = jnp.concatenate([cot, after], axis=0)
    grad_act, grad_tw = temporal_back(act, later, temporal_w)
    sig = jax.nn.sigmoid(pre)
    grad_pre = (grad_act.astype(jnp.float32) * sig * (1.0 + pre * (1.0 - sig))).astype(jnp.bfloat16)
    grad_in = (cot.astype(jnp.float32) + spatial_transpose(grad_pre, spatial_w)).astype(
        jnp.bfloat16
    )
    grad_sw = spatial_weight_grad(frames, grad_pre)
    grad_sb = jnp.sum(grad_pre.astype(jnp.float32).reshape(-1, chan), axis=0)
    n_sw = 9 * chan
    n_tw = 3 * chan
    rows = n_sw + n_tw + 1
    quantum = 64
    padded_rows = -(-rows // quantum) * quantum
    packed = jnp.concatenate(
        [
            grad_sw.reshape(n_sw, chan),
            grad_tw.reshape(n_tw, chan),
            grad_sb[None],
            jnp.zeros((padded_rows - rows, chan), jnp.float32),
        ],
        axis=0,
    )
    total = all_reduce(packed, n_clip, n_tm)
    total_cells = n_clip * count * n_tm * height * width
    norm = 1.0 / jnp.sqrt(jnp.float32(total_cells))
    out_sw = total[:n_sw].reshape(3, 3, chan, chan) * norm
    out_tw = total[n_sw : n_sw + n_tw].reshape(3, chan, chan) * norm
    out_sb = total[n_sw + n_tw] * norm
    return (grad_in[None], out_sw, out_sb, out_tw)


def solution(mesh):
    in_specs = (P("clip", "tm", None, None, None), P("clip", "tm", None, None, None), P(), P(), P())
    out_specs = (P("clip", "tm", None, None, None), P(), P(), P())
    return jax.shard_map(local, mesh=mesh, in_specs=in_specs, out_specs=out_specs, check_vma=False)
```

```python
import jax
import jax.numpy as jnp
from jax import lax
from jax.sharding import PartitionSpec as P

GRAY4 = (0, 1, 3, 2)


CONV_DIMS = ("NHWC", "HWIO", "NHWC")


def spatial_forward(frames, weights, bias):
    total = lax.conv_general_dilated(
        frames, weights, (1, 1), ((1, 1), (1, 1)), dimension_numbers=CONV_DIMS,
        preferred_element_type=jnp.float32,
    )
    return total + bias


def spatial_transpose(grads, weights):
    flipped = jnp.transpose(weights[::-1, ::-1], (0, 1, 3, 2))
    return lax.conv_general_dilated(
        grads, flipped, (1, 1), ((1, 1), (1, 1)), dimension_numbers=CONV_DIMS,
        preferred_element_type=jnp.float32,
    )


def spatial_weight_grad(frames, grads):
    result = lax.conv_general_dilated(
        frames, grads, (1, 1), ((1, 1), (1, 1)), dimension_numbers=("CHWN", "IHWO", "NHWC"),
        preferred_element_type=jnp.float32,
    )
    return jnp.transpose(result, (1, 2, 0, 3))


def temporal_back(act, later, temporal_w):
    count, height, width, chan = act.shape
    flat_act = act.reshape(-1, chan)
    grad_act = jnp.zeros((count * height * width, chan), jnp.float32)
    lag_terms = []
    for k in range(3):
        window = later[k : k + count].reshape(-1, chan)
        grad_act = grad_act + jnp.dot(window, temporal_w[k].T, preferred_element_type=jnp.float32)
        lag_terms.append(
            lax.dot_general(
                flat_act, window, (((0,), (0,)), ((), ())), preferred_element_type=jnp.float32
            )
        )
    grad_act = grad_act.astype(jnp.bfloat16).reshape(count, height, width, chan)
    return grad_act, jnp.stack(lag_terms)


ZRING = (2, 0, 8, 11, 3, 1, 9, 15, 7, 13, 5, 14, 6, 12, 4, 10)


def butterfly_steps(n_clip, n_tm):
    n_x = n_clip // 16
    steps = []

    def clip_step(size, stride, labels, bit, kind):
        perm, bits = [], []
        pos = {lab: r for r, lab in enumerate(labels)}
        for c in range(n_clip):
            r = (c // stride) % size
            lab = labels[r]
            r2 = pos[lab ^ (1 << bit)]
            perm.append((c, c + (r2 - r) * stride))
            bits.append((lab >> bit) & 1)
        steps.append(("clip", tuple(perm), tuple(bits), kind))

    clip_step(2, 1, (0, 1), 0, "halve")
    for b in range(2):
        clip_step(n_x, 16, GRAY4, b, "halve")
    for b in range(2):
        clip_step(4, 4, GRAY4, b, "add")
    pos = {lab: p for p, lab in enumerate(ZRING)}
    for b in range(4):
        perm = []
        for c in range(n_clip):
            zh = (c // 2) % 2
            for t in range(n_tm):
                p2 = pos[ZRING[zh * n_tm + t] ^ (1 << b)]
                c2 = c + (p2 // n_tm - zh) * 2
                perm.append((c * n_tm + t, c2 * n_tm + p2 % n_tm))
        steps.append((("clip", "tm"), tuple(perm), None, "add"))
    return steps


def all_reduce(x, n_clip, n_tm):
    steps = butterfly_steps(n_clip, n_tm)
    halved = []
    for axis, perm, bits, kind in steps:
        if kind == "halve":
            bit = jnp.asarray(bits, jnp.int32)[lax.axis_index(axis)]
            h = x.shape[0] // 2
            keep = lax.dynamic_slice_in_dim(x, bit * h, h)
            send = lax.dynamic_slice_in_dim(x, (1 - bit) * h, h)
            x = keep + lax.ppermute(send, axis, perm)
            halved.append((axis, perm, bits))
        else:
            x = x + lax.ppermute(x, axis, perm)
    for axis, perm, bits in halved[::-1]:
        bit = jnp.asarray(bits, jnp.int32)[lax.axis_index(axis)]
        other = lax.ppermute(x, axis, perm)
        both = jnp.stack([x, other])
        first = lax.dynamic_index_in_dim(both, bit, keepdims=False)
        second = lax.dynamic_index_in_dim(both, 1 - bit, keepdims=False)
        x = jnp.concatenate([first, second], 0)
    return x


def local(clip_in, cotangent, spatial_w, spatial_b, temporal_w):
    frames = clip_in[0]
    cot = cotangent[0]
    count, height, width, chan = frames.shape
    n_tm = lax.axis_size("tm")
    n_clip = lax.axis_size("clip")
    after = lax.ppermute(cot, "tm", [(t, t - 1) for t in range(1, n_tm)])
    pre = spatial_forward(frames, spatial_w, spatial_b)
    act = jax.nn.silu(pre).astype(jnp.bfloat16)
    later = jnp.concatenate([cot, after], axis=0)
    grad_act, grad_tw = temporal_back(act, later, temporal_w)
    sig = jax.nn.sigmoid(pre)
    grad_pre = (grad_act.astype(jnp.float32) * sig * (1.0 + pre * (1.0 - sig))).astype(jnp.bfloat16)
    grad_in = (cot.astype(jnp.float32) + spatial_transpose(grad_pre, spatial_w)).astype(
        jnp.bfloat16
    )
    grad_sw = spatial_weight_grad(frames, grad_pre)
    grad_sb = jnp.sum(grad_pre.astype(jnp.float32).reshape(-1, chan), axis=0)
    n_sw = 9 * chan
    n_tw = 3 * chan
    rows = n_sw + n_tw + 1
    quantum = 64
    padded_rows = -(-rows // quantum) * quantum
    packed = jnp.concatenate(
        [
            grad_sw.reshape(n_sw, chan),
            grad_tw.reshape(n_tw, chan),
            grad_sb[None],
            jnp.zeros((padded_rows - rows, chan), jnp.float32),
        ],
        axis=0,
    )
    total = all_reduce(packed, n_clip, n_tm)
    total_cells = n_clip * count * n_tm * height * width
    norm = 1.0 / jnp.sqrt(jnp.float32(total_cells))
    out_sw = total[:n_sw].reshape(3, 3, chan, chan) * norm
    out_tw = total[n_sw : n_sw + n_tw].reshape(3, chan, chan) * norm
    out_sb = total[n_sw + n_tw] * norm
    return (grad_in[None], out_sw, out_sb, out_tw)


def solution(mesh):
    in_specs = (P("clip", "tm", None, None, None), P("clip", "tm", None, None, None), P(), P(), P())
    out_specs = (P("clip", "tm", None, None, None), P(), P(), P())
    return jax.shard_map(local, mesh=mesh, in_specs=in_specs, out_specs=out_specs, check_vma=False)
```

```python
import jax
import jax.numpy as jnp
from jax import lax
from jax.sharding import PartitionSpec as P

GRAY4 = (0, 1, 3, 2)


CONV_DIMS = ("NHWC", "HWIO", "NHWC")


def spatial_forward(frames, weights, bias):
    total = lax.conv_general_dilated(
        frames, weights, (1, 1), ((1, 1), (1, 1)), dimension_numbers=CONV_DIMS,
        preferred_element_type=jnp.float32,
    )
    return total + bias


def spatial_transpose(grads, weights):
    flipped = jnp.transpose(weights[::-1, ::-1], (0, 1, 3, 2))
    return lax.conv_general_dilated(
        grads, flipped, (1, 1), ((1, 1), (1, 1)), dimension_numbers=CONV_DIMS,
        preferred_element_type=jnp.float32,
    )


def spatial_weight_grad(frames, grads):
    result = lax.conv_general_dilated(
        frames, grads, (1, 1), ((1, 1), (1, 1)), dimension_numbers=("CHWN", "IHWO", "NHWC"),
        preferred_element_type=jnp.float32,
    )
    return jnp.transpose(result, (1, 2, 0, 3))


def temporal_back(act, later, temporal_w):
    count, height, width, chan = act.shape
    flat_act = act.reshape(-1, chan)
    grad_act = jnp.zeros((count * height * width, chan), jnp.float32)
    lag_terms = []
    for k in range(3):
        window = later[k : k + count].reshape(-1, chan)
        grad_act = grad_act + jnp.dot(window, temporal_w[k].T, preferred_element_type=jnp.float32)
        lag_terms.append(
            lax.dot_general(
                flat_act, window, (((0,), (0,)), ((), ())), preferred_element_type=jnp.float32
            )
        )
    grad_act = grad_act.astype(jnp.bfloat16).reshape(count, height, width, chan)
    return grad_act, jnp.stack(lag_terms)


ZRING = (0, 1, 3, 2, 4, 5, 7, 6, 12, 13, 15, 14, 8, 9, 11, 10)


def butterfly_steps(n_clip, n_tm):
    n_x = n_clip // 16
    steps = []

    def clip_step(size, stride, labels, bit, kind):
        perm, bits = [], []
        pos = {lab: r for r, lab in enumerate(labels)}
        for c in range(n_clip):
            r = (c // stride) % size
            lab = labels[r]
            r2 = pos[lab ^ (1 << bit)]
            perm.append((c, c + (r2 - r) * stride))
            bits.append((lab >> bit) & 1)
        steps.append(("clip", tuple(perm), tuple(bits), kind))

    clip_step(2, 1, (0, 1), 0, "halve")
    for b in range(2):
        clip_step(n_x, 16, GRAY4, b, "halve")
    for b in range(2):
        clip_step(4, 4, GRAY4, b, "add")
    pos = {lab: p for p, lab in enumerate(ZRING)}
    for b in range(4):
        perm = []
        for c in range(n_clip):
            zh = (c // 2) % 2
            for t in range(n_tm):
                p2 = pos[ZRING[zh * n_tm + t] ^ (1 << b)]
                c2 = c + (p2 // n_tm - zh) * 2
                perm.append((c * n_tm + t, c2 * n_tm + p2 % n_tm))
        steps.append((("clip", "tm"), tuple(perm), None, "add"))
    return steps


def all_reduce(x, n_clip, n_tm):
    steps = butterfly_steps(n_clip, n_tm)
    halved = []
    for axis, perm, bits, kind in steps:
        if kind == "halve":
            bit = jnp.asarray(bits, jnp.int32)[lax.axis_index(axis)]
            h = x.shape[0] // 2
            keep = lax.dynamic_slice_in_dim(x, bit * h, h)
            send = lax.dynamic_slice_in_dim(x, (1 - bit) * h, h)
            x = keep + lax.ppermute(send, axis, perm)
            halved.append((axis, perm, bits))
        else:
            x = x + lax.ppermute(x, axis, perm)
    for axis, perm, bits in halved[::-1]:
        bit = jnp.asarray(bits, jnp.int32)[lax.axis_index(axis)]
        other = lax.ppermute(x, axis, perm)
        both = jnp.stack([x, other])
        first = lax.dynamic_index_in_dim(both, bit, keepdims=False)
        second = lax.dynamic_index_in_dim(both, 1 - bit, keepdims=False)
        x = jnp.concatenate([first, second], 0)
    return x


def local(clip_in, cotangent, spatial_w, spatial_b, temporal_w):
    frames = clip_in[0]
    cot = cotangent[0]
    count, height, width, chan = frames.shape
    n_tm = lax.axis_size("tm")
    n_clip = lax.axis_size("clip")
    after = lax.ppermute(cot, "tm", [(t, t - 1) for t in range(1, n_tm)])
    pre = spatial_forward(frames, spatial_w, spatial_b)
    act = jax.nn.silu(pre).astype(jnp.bfloat16)
    later = jnp.concatenate([cot, after], axis=0)
    grad_act, grad_tw = temporal_back(act, later, temporal_w)
    sig = jax.nn.sigmoid(pre)
    grad_pre = (grad_act.astype(jnp.float32) * sig * (1.0 + pre * (1.0 - sig))).astype(jnp.bfloat16)
    grad_in = (cot.astype(jnp.float32) + spatial_transpose(grad_pre, spatial_w)).astype(
        jnp.bfloat16
    )
    grad_sw = spatial_weight_grad(frames, grad_pre)
    grad_sb = jnp.sum(grad_pre.astype(jnp.float32).reshape(-1, chan), axis=0)
    n_sw = 9 * chan
    n_tw = 3 * chan
    rows = n_sw + n_tw + 1
    quantum = 64
    padded_rows = -(-rows // quantum) * quantum
    packed = jnp.concatenate(
        [
            grad_sw.reshape(n_sw, chan),
            grad_tw.reshape(n_tw, chan),
            grad_sb[None],
            jnp.zeros((padded_rows - rows, chan), jnp.float32),
        ],
        axis=0,
    )
    total = all_reduce(packed, n_clip, n_tm)
    total_cells = n_clip * count * n_tm * height * width
    norm = 1.0 / jnp.sqrt(jnp.float32(total_cells))
    out_sw = total[:n_sw].reshape(3, 3, chan, chan) * norm
    out_tw = total[n_sw : n_sw + n_tw].reshape(3, chan, chan) * norm
    out_sb = total[n_sw + n_tw] * norm
    return (grad_in[None], out_sw, out_sb, out_tw)


def solution(mesh):
    in_specs = (P("clip", "tm", None, None, None), P("clip", "tm", None, None, None), P(), P(), P())
    out_specs = (P("clip", "tm", None, None, None), P(), P(), P())
    return jax.shard_map(local, mesh=mesh, in_specs=in_specs, out_specs=out_specs, check_vma=False)
```

```python
import jax
import jax.numpy as jnp
from jax import lax
from jax.sharding import PartitionSpec as P

GRAY4 = (0, 1, 3, 2)


CONV_DIMS = ("NHWC", "HWIO", "NHWC")


def spatial_forward(frames, weights, bias):
    total = lax.conv_general_dilated(
        frames, weights, (1, 1), ((1, 1), (1, 1)), dimension_numbers=CONV_DIMS,
        preferred_element_type=jnp.float32,
    )
    return total + bias


def spatial_transpose(grads, weights):
    flipped = jnp.transpose(weights[::-1, ::-1], (0, 1, 3, 2))
    return lax.conv_general_dilated(
        grads, flipped, (1, 1), ((1, 1), (1, 1)), dimension_numbers=CONV_DIMS,
        preferred_element_type=jnp.float32,
    )


def spatial_weight_grad(frames, grads):
    result = lax.conv_general_dilated(
        frames, grads, (1, 1), ((1, 1), (1, 1)), dimension_numbers=("CHWN", "IHWO", "NHWC"),
        preferred_element_type=jnp.float32,
    )
    return jnp.transpose(result, (1, 2, 0, 3))


def temporal_back(act, later, temporal_w):
    count, height, width, chan = act.shape
    flat_act = act.reshape(-1, chan)
    grad_act = jnp.zeros((count * height * width, chan), jnp.float32)
    lag_terms = []
    for k in range(3):
        window = later[k : k + count].reshape(-1, chan)
        grad_act = grad_act + jnp.dot(window, temporal_w[k].T, preferred_element_type=jnp.float32)
        lag_terms.append(
            lax.dot_general(
                flat_act, window, (((0,), (0,)), ((), ())), preferred_element_type=jnp.float32
            )
        )
    grad_act = grad_act.astype(jnp.bfloat16).reshape(count, height, width, chan)
    return grad_act, jnp.stack(lag_terms)


ZRING = (0, 1, 3, 2, 4, 5, 7, 6, 12, 13, 15, 14, 8, 9, 11, 10)


def butterfly_steps(n_clip, n_tm):
    n_x = n_clip // 16
    steps = []

    def clip_step(size, stride, labels, bit, kind):
        perm = []
        pos = {lab: r for r, lab in enumerate(labels)}
        for c in range(n_clip):
            r = (c // stride) % size
            lab = labels[r]
            r2 = pos[lab ^ (1 << bit)]
            perm.append((c, c + (r2 - r) * stride))
        steps.append(("clip", tuple(perm), (stride, size, labels is GRAY4, bit), kind))

    clip_step(2, 1, (0, 1), 0, "halve")
    for b in range(2):
        clip_step(n_x, 16, GRAY4, b, "halve")
    for b in range(2):
        clip_step(4, 4, GRAY4, b, "add")
    pos = {lab: p for p, lab in enumerate(ZRING)}
    for b in range(4):
        perm = []
        for c in range(n_clip):
            zh = (c // 2) % 2
            for t in range(n_tm):
                p2 = pos[ZRING[zh * n_tm + t] ^ (1 << b)]
                c2 = c + (p2 // n_tm - zh) * 2
                perm.append((c * n_tm + t, c2 * n_tm + p2 % n_tm))
        steps.append((("clip", "tm"), tuple(perm), None, "add"))
    return steps


def label_bit(axis, where):
    stride, size, gray, bit = where
    r = (lax.axis_index(axis) // stride) % size
    if gray:
        r = r ^ (r >> 1)
    return (r >> bit) & 1


def all_reduce(x, n_clip, n_tm):
    steps = butterfly_steps(n_clip, n_tm)
    halved = []
    for axis, perm, bits, kind in steps:
        if kind == "halve":
            bit = label_bit(axis, bits)
            h = x.shape[0] // 2
            keep = lax.dynamic_slice_in_dim(x, bit * h, h)
            send = lax.dynamic_slice_in_dim(x, (1 - bit) * h, h)
            x = keep + lax.ppermute(send, axis, perm)
            halved.append((axis, perm, bits))
        else:
            x = x + lax.ppermute(x, axis, perm)
    for axis, perm, bits in halved[::-1]:
        bit = label_bit(axis, bits)
        other = lax.ppermute(x, axis, perm)
        both = jnp.stack([x, other])
        first = lax.dynamic_index_in_dim(both, bit, keepdims=False)
        second = lax.dynamic_index_in_dim(both, 1 - bit, keepdims=False)
        x = jnp.concatenate([first, second], 0)
    return x


def local(clip_in, cotangent, spatial_w, spatial_b, temporal_w):
    frames = clip_in[0]
    cot = cotangent[0]
    count, height, width, chan = frames.shape
    n_tm = lax.axis_size("tm")
    n_clip = lax.axis_size("clip")
    after = lax.ppermute(cot, "tm", [(t, t - 1) for t in range(1, n_tm)])
    pre = spatial_forward(frames, spatial_w, spatial_b)
    act = jax.nn.silu(pre).astype(jnp.bfloat16)
    later = jnp.concatenate([cot, after], axis=0)
    grad_act, grad_tw = temporal_back(act, later, temporal_w)
    sig = jax.nn.sigmoid(pre)
    grad_pre = (grad_act.astype(jnp.float32) * sig * (1.0 + pre * (1.0 - sig))).astype(jnp.bfloat16)
    grad_in = (cot.astype(jnp.float32) + spatial_transpose(grad_pre, spatial_w)).astype(
        jnp.bfloat16
    )
    grad_sw = spatial_weight_grad(frames, grad_pre)
    grad_sb = jnp.sum(grad_pre.astype(jnp.float32).reshape(-1, chan), axis=0)
    n_sw = 9 * chan
    n_tw = 3 * chan
    rows = n_sw + n_tw + 1
    quantum = 64
    padded_rows = -(-rows // quantum) * quantum
    packed = jnp.concatenate(
        [
            grad_sw.reshape(n_sw, chan),
            grad_tw.reshape(n_tw, chan),
            grad_sb[None],
            jnp.zeros((padded_rows - rows, chan), jnp.float32),
        ],
        axis=0,
    )
    total = all_reduce(packed, n_clip, n_tm)
    total_cells = n_clip * count * n_tm * height * width
    norm = 1.0 / jnp.sqrt(jnp.float32(total_cells))
    out_sw = total[:n_sw].reshape(3, 3, chan, chan) * norm
    out_tw = total[n_sw : n_sw + n_tw].reshape(3, chan, chan) * norm
    out_sb = total[n_sw + n_tw] * norm
    return (grad_in[None], out_sw, out_sb, out_tw)


def solution(mesh):
    in_specs = (P("clip", "tm", None, None, None), P("clip", "tm", None, None, None), P(), P(), P())
    out_specs = (P("clip", "tm", None, None, None), P(), P(), P())
    return jax.shard_map(local, mesh=mesh, in_specs=in_specs, out_specs=out_specs, check_vma=False)
```

```python
import jax
import jax.numpy as jnp
from jax import lax
from jax.sharding import PartitionSpec as P

GRAY4 = (0, 1, 3, 2)


CONV_DIMS = ("NHWC", "HWIO", "NHWC")


def spatial_forward(frames, weights, bias):
    total = lax.conv_general_dilated(
        frames, weights, (1, 1), ((1, 1), (1, 1)), dimension_numbers=CONV_DIMS,
        preferred_element_type=jnp.float32,
    )
    return total + bias


def spatial_transpose(grads, weights):
    flipped = jnp.transpose(weights[::-1, ::-1], (0, 1, 3, 2))
    return lax.conv_general_dilated(
        grads, flipped, (1, 1), ((1, 1), (1, 1)), dimension_numbers=CONV_DIMS,
        preferred_element_type=jnp.float32,
    )


def spatial_weight_grad(frames, grads):
    result = lax.conv_general_dilated(
        frames, grads, (1, 1), ((1, 1), (1, 1)), dimension_numbers=("CHWN", "IHWO", "NHWC"),
        preferred_element_type=jnp.float32,
    )
    return jnp.transpose(result, (1, 2, 0, 3))


def temporal_back(act, later, temporal_w):
    count, height, width, chan = act.shape
    flat_act = act.reshape(-1, chan)
    grad_act = jnp.zeros((count * height * width, chan), jnp.float32)
    lag_terms = []
    for k in range(3):
        window = later[k : k + count].reshape(-1, chan)
        grad_act = grad_act + jnp.dot(window, temporal_w[k].T, preferred_element_type=jnp.float32)
        lag_terms.append(
            lax.dot_general(
                flat_act, window, (((0,), (0,)), ((), ())), preferred_element_type=jnp.float32
            )
        )
    grad_act = grad_act.astype(jnp.bfloat16).reshape(count, height, width, chan)
    return grad_act, jnp.stack(lag_terms)


ZRING = (0, 1, 3, 2, 4, 5, 7, 6, 12, 13, 15, 14, 8, 9, 11, 10)


def butterfly_steps(n_clip, n_tm):
    n_x = n_clip // 16
    steps = []

    def clip_step(size, stride, labels, bit, kind):
        perm = []
        pos = {lab: r for r, lab in enumerate(labels)}
        for c in range(n_clip):
            r = (c // stride) % size
            lab = labels[r]
            r2 = pos[lab ^ (1 << bit)]
            perm.append((c, c + (r2 - r) * stride))
        steps.append(("clip", tuple(perm), (stride, size, labels is GRAY4, bit), kind))

    clip_step(2, 1, (0, 1), 0, "halve")
    for b in range(2):
        clip_step(n_x, 16, GRAY4, b, "halve")
    for b in range(2):
        clip_step(4, 4, GRAY4, b, "add")
    pos = {lab: p for p, lab in enumerate(ZRING)}
    for b in (3, 2, 1, 0):
        perm = []
        for c in range(n_clip):
            zh = (c // 2) % 2
            for t in range(n_tm):
                p2 = pos[ZRING[zh * n_tm + t] ^ (1 << b)]
                c2 = c + (p2 // n_tm - zh) * 2
                perm.append((c * n_tm + t, c2 * n_tm + p2 % n_tm))
        steps.append((("clip", "tm"), tuple(perm), None, "add"))
    return steps


def label_bit(axis, where):
    stride, size, gray, bit = where
    r = (lax.axis_index(axis) // stride) % size
    if gray:
        r = r ^ (r >> 1)
    return (r >> bit) & 1


def all_reduce(x, n_clip, n_tm):
    steps = butterfly_steps(n_clip, n_tm)
    halved = []
    for axis, perm, bits, kind in steps:
        if kind == "halve":
            bit = label_bit(axis, bits)
            h = x.shape[0] // 2
            keep = lax.dynamic_slice_in_dim(x, bit * h, h)
            send = lax.dynamic_slice_in_dim(x, (1 - bit) * h, h)
            x = keep + lax.ppermute(send, axis, perm)
            halved.append((axis, perm, bits))
        else:
            x = x + lax.ppermute(x, axis, perm)
    for axis, perm, bits in halved[::-1]:
        bit = label_bit(axis, bits)
        other = lax.ppermute(x, axis, perm)
        both = jnp.stack([x, other])
        first = lax.dynamic_index_in_dim(both, bit, keepdims=False)
        second = lax.dynamic_index_in_dim(both, 1 - bit, keepdims=False)
        x = jnp.concatenate([first, second], 0)
    return x


def local(clip_in, cotangent, spatial_w, spatial_b, temporal_w):
    frames = clip_in[0]
    cot = cotangent[0]
    count, height, width, chan = frames.shape
    n_tm = lax.axis_size("tm")
    n_clip = lax.axis_size("clip")
    after = lax.ppermute(cot, "tm", [(t, t - 1) for t in range(1, n_tm)])
    pre = spatial_forward(frames, spatial_w, spatial_b)
    act = jax.nn.silu(pre).astype(jnp.bfloat16)
    later = jnp.concatenate([cot, after], axis=0)
    grad_act, grad_tw = temporal_back(act, later, temporal_w)
    sig = jax.nn.sigmoid(pre)
    grad_pre = (grad_act.astype(jnp.float32) * sig * (1.0 + pre * (1.0 - sig))).astype(jnp.bfloat16)
    grad_in = (cot.astype(jnp.float32) + spatial_transpose(grad_pre, spatial_w)).astype(
        jnp.bfloat16
    )
    grad_sw = spatial_weight_grad(frames, grad_pre)
    grad_sb = jnp.sum(grad_pre.astype(jnp.float32).reshape(-1, chan), axis=0)
    n_sw = 9 * chan
    n_tw = 3 * chan
    rows = n_sw + n_tw + 1
    quantum = 64
    padded_rows = -(-rows // quantum) * quantum
    packed = jnp.concatenate(
        [
            grad_sw.reshape(n_sw, chan),
            grad_tw.reshape(n_tw, chan),
            grad_sb[None],
            jnp.zeros((padded_rows - rows, chan), jnp.float32),
        ],
        axis=0,
    )
    total = all_reduce(packed, n_clip, n_tm)
    total_cells = n_clip * count * n_tm * height * width
    norm = 1.0 / jnp.sqrt(jnp.float32(total_cells))
    out_sw = total[:n_sw].reshape(3, 3, chan, chan) * norm
    out_tw = total[n_sw : n_sw + n_tw].reshape(3, chan, chan) * norm
    out_sb = total[n_sw + n_tw] * norm
    return (grad_in[None], out_sw, out_sb, out_tw)


def solution(mesh):
    in_specs = (P("clip", "tm", None, None, None), P("clip", "tm", None, None, None), P(), P(), P())
    out_specs = (P("clip", "tm", None, None, None), P(), P(), P())
    return jax.shard_map(local, mesh=mesh, in_specs=in_specs, out_specs=out_specs, check_vma=False)
```

```python
import jax
import jax.numpy as jnp
from jax import lax
from jax.sharding import PartitionSpec as P

GRAY4 = (0, 1, 3, 2)


CONV_DIMS = ("NHWC", "HWIO", "NHWC")


def spatial_forward(frames, weights, bias):
    total = lax.conv_general_dilated(
        frames, weights, (1, 1), ((1, 1), (1, 1)), dimension_numbers=CONV_DIMS,
        preferred_element_type=jnp.float32,
    )
    return total + bias


def spatial_transpose(grads, weights):
    flipped = jnp.transpose(weights[::-1, ::-1], (0, 1, 3, 2))
    return lax.conv_general_dilated(
        grads, flipped, (1, 1), ((1, 1), (1, 1)), dimension_numbers=CONV_DIMS,
        preferred_element_type=jnp.float32,
    )


def spatial_weight_grad(frames, grads):
    count, height, width, chan = frames.shape
    padded = jnp.pad(frames, ((0, 0), (1, 1), (1, 1), (0, 0)))
    flat_grads = grads.reshape(-1, chan)
    result = []
    for i in range(3):
        row_terms = []
        for j in range(3):
            window = padded[:, i : i + height, j : j + width, :].reshape(-1, chan)
            row_terms.append(
                lax.dot_general(
                    window, flat_grads, (((0,), (0,)), ((), ())), preferred_element_type=jnp.float32
                )
            )
        result.append(jnp.stack(row_terms))
    return jnp.stack(result)


def temporal_back(act, later, temporal_w):
    count, height, width, chan = act.shape
    flat_act = act.reshape(-1, chan)
    grad_act = jnp.zeros((count * height * width, chan), jnp.float32)
    lag_terms = []
    for k in range(3):
        window = later[k : k + count].reshape(-1, chan)
        grad_act = grad_act + jnp.dot(window, temporal_w[k].T, preferred_element_type=jnp.float32)
        lag_terms.append(
            lax.dot_general(
                flat_act, window, (((0,), (0,)), ((), ())), preferred_element_type=jnp.float32
            )
        )
    grad_act = grad_act.astype(jnp.bfloat16).reshape(count, height, width, chan)
    return grad_act, jnp.stack(lag_terms)


ZRING = (0, 1, 3, 2, 4, 5, 7, 6, 12, 13, 15, 14, 8, 9, 11, 10)


def butterfly_steps(n_clip, n_tm):
    n_x = n_clip // 16
    steps = []

    def clip_step(size, stride, labels, bit, kind):
        perm = []
        pos = {lab: r for r, lab in enumerate(labels)}
        for c in range(n_clip):
            r = (c // stride) % size
            lab = labels[r]
            r2 = pos[lab ^ (1 << bit)]
            perm.append((c, c + (r2 - r) * stride))
        steps.append(("clip", tuple(perm), (stride, size, labels is GRAY4, bit), kind))

    clip_step(2, 1, (0, 1), 0, "halve")
    for b in range(2):
        clip_step(n_x, 16, GRAY4, b, "halve")
    for b in range(2):
        clip_step(4, 4, GRAY4, b, "add")
    pos = {lab: p for p, lab in enumerate(ZRING)}
    for b in range(4):
        perm = []
        for c in range(n_clip):
            zh = (c // 2) % 2
            for t in range(n_tm):
                p2 = pos[ZRING[zh * n_tm + t] ^ (1 << b)]
                c2 = c + (p2 // n_tm - zh) * 2
                perm.append((c * n_tm + t, c2 * n_tm + p2 % n_tm))
        steps.append((("clip", "tm"), tuple(perm), None, "add"))
    return steps


def label_bit(axis, where):
    stride, size, gray, bit = where
    r = (lax.axis_index(axis) // stride) % size
    if gray:
        r = r ^ (r >> 1)
    return (r >> bit) & 1


def all_reduce(x, n_clip, n_tm):
    steps = butterfly_steps(n_clip, n_tm)
    halved = []
    for axis, perm, bits, kind in steps:
        if kind == "halve":
            bit = label_bit(axis, bits)
            h = x.shape[0] // 2
            keep = lax.dynamic_slice_in_dim(x, bit * h, h)
            send = lax.dynamic_slice_in_dim(x, (1 - bit) * h, h)
            x = keep + lax.ppermute(send, axis, perm)
            halved.append((axis, perm, bits))
        else:
            x = x + lax.ppermute(x, axis, perm)
    for axis, perm, bits in halved[::-1]:
        bit = label_bit(axis, bits)
        other = lax.ppermute(x, axis, perm)
        both = jnp.stack([x, other])
        first = lax.dynamic_index_in_dim(both, bit, keepdims=False)
        second = lax.dynamic_index_in_dim(both, 1 - bit, keepdims=False)
        x = jnp.concatenate([first, second], 0)
    return x


def local(clip_in, cotangent, spatial_w, spatial_b, temporal_w):
    frames = clip_in[0]
    cot = cotangent[0]
    count, height, width, chan = frames.shape
    n_tm = lax.axis_size("tm")
    n_clip = lax.axis_size("clip")
    after = lax.ppermute(cot, "tm", [(t, t - 1) for t in range(1, n_tm)])
    pre = spatial_forward(frames, spatial_w, spatial_b)
    act = jax.nn.silu(pre).astype(jnp.bfloat16)
    later = jnp.concatenate([cot, after], axis=0)
    grad_act, grad_tw = temporal_back(act, later, temporal_w)
    sig = jax.nn.sigmoid(pre)
    grad_pre = (grad_act.astype(jnp.float32) * sig * (1.0 + pre * (1.0 - sig))).astype(jnp.bfloat16)
    grad_in = (cot.astype(jnp.float32) + spatial_transpose(grad_pre, spatial_w)).astype(
        jnp.bfloat16
    )
    grad_sw = spatial_weight_grad(frames, grad_pre)
    grad_sb = jnp.sum(grad_pre.astype(jnp.float32).reshape(-1, chan), axis=0)
    n_sw = 9 * chan
    n_tw = 3 * chan
    rows = n_sw + n_tw + 1
    quantum = 64
    padded_rows = -(-rows // quantum) * quantum
    packed = jnp.concatenate(
        [
            grad_sw.reshape(n_sw, chan),
            grad_tw.reshape(n_tw, chan),
            grad_sb[None],
            jnp.zeros((padded_rows - rows, chan), jnp.float32),
        ],
        axis=0,
    )
    total = all_reduce(packed, n_clip, n_tm)
    total_cells = n_clip * count * n_tm * height * width
    norm = 1.0 / jnp.sqrt(jnp.float32(total_cells))
    out_sw = total[:n_sw].reshape(3, 3, chan, chan) * norm
    out_tw = total[n_sw : n_sw + n_tw].reshape(3, chan, chan) * norm
    out_sb = total[n_sw + n_tw] * norm
    return (grad_in[None], out_sw, out_sb, out_tw)


def solution(mesh):
    in_specs = (P("clip", "tm", None, None, None), P("clip", "tm", None, None, None), P(), P(), P())
    out_specs = (P("clip", "tm", None, None, None), P(), P(), P())
    return jax.shard_map(local, mesh=mesh, in_specs=in_specs, out_specs=out_specs, check_vma=False)
```

```python
import jax
import jax.numpy as jnp
from jax import lax
from jax.sharding import PartitionSpec as P

GRAY4 = (0, 1, 3, 2)


CONV_DIMS = ("NHWC", "HWIO", "NHWC")


def spatial_forward(frames, weights, bias):
    total = lax.conv_general_dilated(
        frames, weights, (1, 1), ((1, 1), (1, 1)), dimension_numbers=CONV_DIMS,
        preferred_element_type=jnp.float32,
    )
    return total + bias


def spatial_transpose(grads, weights):
    flipped = jnp.transpose(weights[::-1, ::-1], (0, 1, 3, 2))
    return lax.conv_general_dilated(
        grads, flipped, (1, 1), ((1, 1), (1, 1)), dimension_numbers=CONV_DIMS,
        preferred_element_type=jnp.float32,
    )


def spatial_weight_grad(frames, grads):
    count, height, width, chan = frames.shape
    padded = jnp.pad(frames, ((0, 0), (1, 1), (1, 1), (0, 0)))
    flat_grads = grads.reshape(-1, chan)
    result = []
    for i in range(3):
        row_terms = []
        for j in range(3):
            window = padded[:, i : i + height, j : j + width, :].reshape(-1, chan)
            row_terms.append(
                lax.dot_general(
                    window, flat_grads, (((0,), (0,)), ((), ())), preferred_element_type=jnp.float32
                )
            )
        result.append(jnp.stack(row_terms))
    return jnp.stack(result)


def temporal_back(act, later, temporal_w):
    count, height, width, chan = act.shape
    flat_act = act.reshape(-1, chan)
    grad_act = jnp.zeros((count * height * width, chan), jnp.float32)
    lag_terms = []
    for k in range(3):
        window = later[k : k + count].reshape(-1, chan)
        grad_act = grad_act + jnp.dot(window, temporal_w[k].T, preferred_element_type=jnp.float32)
        lag_terms.append(
            lax.dot_general(
                flat_act, window, (((0,), (0,)), ((), ())), preferred_element_type=jnp.float32
            )
        )
    grad_act = grad_act.astype(jnp.bfloat16).reshape(count, height, width, chan)
    return grad_act, jnp.stack(lag_terms)


ZRING = (0, 1, 3, 2, 4, 5, 7, 6, 12, 13, 15, 14, 8, 9, 11, 10)


def butterfly_steps(n_clip, n_tm):
    n_x = n_clip // 16
    steps = []

    def clip_step(size, stride, labels, bit, kind):
        perm = []
        pos = {lab: r for r, lab in enumerate(labels)}
        for c in range(n_clip):
            r = (c // stride) % size
            lab = labels[r]
            r2 = pos[lab ^ (1 << bit)]
            perm.append((c, c + (r2 - r) * stride))
        steps.append(("clip", tuple(perm), (stride, size, labels is GRAY4, bit), kind))

    clip_step(2, 1, (0, 1), 0, "halve")
    for b in range(2):
        clip_step(n_x, 16, GRAY4, b, "halve")
    for b in range(2):
        clip_step(4, 4, GRAY4, b, "add")
    pos = {lab: p for p, lab in enumerate(ZRING)}
    for b in range(4):
        perm = []
        for c in range(n_clip):
            zh = (c // 2) % 2
            for t in range(n_tm):
                p2 = pos[ZRING[zh * n_tm + t] ^ (1 << b)]
                c2 = c + (p2 // n_tm - zh) * 2
                perm.append((c * n_tm + t, c2 * n_tm + p2 % n_tm))
        steps.append((("clip", "tm"), tuple(perm), None, "add"))
    return steps


def label_bit(axis, where):
    stride, size, gray, bit = where
    r = (lax.axis_index(axis) // stride) % size
    if gray:
        r = r ^ (r >> 1)
    return (r >> bit) & 1


def all_reduce(x, n_clip, n_tm):
    steps = butterfly_steps(n_clip, n_tm)
    halved = []
    for axis, perm, bits, kind in steps:
        if kind == "halve":
            bit = label_bit(axis, bits)
            h = x.shape[0] // 2
            keep = lax.dynamic_slice_in_dim(x, bit * h, h)
            send = lax.dynamic_slice_in_dim(x, (1 - bit) * h, h)
            x = keep + lax.ppermute(send, axis, perm)
            halved.append((axis, perm, bits))
        else:
            x = x + lax.ppermute(x, axis, perm)
    for axis, perm, bits in halved[::-1]:
        bit = label_bit(axis, bits)
        other = lax.ppermute(x, axis, perm)
        both = jnp.stack([x, other])
        first = lax.dynamic_index_in_dim(both, bit, keepdims=False)
        second = lax.dynamic_index_in_dim(both, 1 - bit, keepdims=False)
        x = jnp.concatenate([first, second], 0)
    return x


def local(clip_in, cotangent, spatial_w, spatial_b, temporal_w):
    frames = clip_in[0]
    cot = cotangent[0]
    count, height, width, chan = frames.shape
    n_tm = lax.axis_size("tm")
    n_clip = lax.axis_size("clip")
    after = lax.ppermute(cot, "tm", [(t, t - 1) for t in range(1, n_tm)])
    pre = spatial_forward(frames, spatial_w, spatial_b)
    act = jax.nn.silu(pre).astype(jnp.bfloat16)
    later = jnp.concatenate([cot, after], axis=0)
    grad_act, grad_tw = temporal_back(act, later, temporal_w)
    sig = jax.nn.sigmoid(pre)
    grad_pre = (grad_act.astype(jnp.float32) * sig * (1.0 + pre * (1.0 - sig))).astype(jnp.bfloat16)
    grad_in = (cot.astype(jnp.float32) + spatial_transpose(grad_pre, spatial_w)).astype(
        jnp.bfloat16
    )
    grad_sw = spatial_weight_grad(frames, grad_pre)
    grad_sb = jnp.sum(grad_pre.astype(jnp.float32).reshape(-1, chan), axis=0)
    n_sw = 9 * chan
    n_tw = 3 * chan
    rows = n_sw + n_tw + 1
    quantum = 8
    padded_rows = -(-rows // quantum) * quantum
    packed = jnp.concatenate(
        [
            grad_sw.reshape(n_sw, chan),
            grad_tw.reshape(n_tw, chan),
            grad_sb[None],
            jnp.zeros((padded_rows - rows, chan), jnp.float32),
        ],
        axis=0,
    )
    total = all_reduce(packed, n_clip, n_tm)
    total_cells = n_clip * count * n_tm * height * width
    norm = 1.0 / jnp.sqrt(jnp.float32(total_cells))
    out_sw = total[:n_sw].reshape(3, 3, chan, chan) * norm
    out_tw = total[n_sw : n_sw + n_tw].reshape(3, chan, chan) * norm
    out_sb = total[n_sw + n_tw] * norm
    return (grad_in[None], out_sw, out_sb, out_tw)


def solution(mesh):
    in_specs = (P("clip", "tm", None, None, None), P("clip", "tm", None, None, None), P(), P(), P())
    out_specs = (P("clip", "tm", None, None, None), P(), P(), P())
    return jax.shard_map(local, mesh=mesh, in_specs=in_specs, out_specs=out_specs, check_vma=False)
```
